256 devices in a mesh: row: 32 (over x_hi, z, core), col: 8 (over y, x_lo).
Axes of the slice: x: 4 (x_hi: 2, x_lo: 2; x = x_hi * 2 + x_lo), y: 4, z: 8, core: 2. Of those that a mesh axis runs over, the one named last changes fastest.
Arguments:
- features: bfloat16 [8, 32, 128, 512], P('col', 'row'), may hold values from -6 to 6
- weight: bfloat16 [512, 512], replicated, may hold values from -0.25 to 0.25
- cotangent: bfloat16 [32, 8, 128, 512], P('row', 'col'), may hold values from -6 to 6
- tile_vals: bfloat16 [32, 8, 128, 128, 128], P('row', 'col'), may hold values from 0 to 1
- tile_rows: int32 [32, 8, 128], P('row', 'col'), may hold values from 0 to 7, as said below
- tile_cols: int32 [32, 8, 128], P('row', 'col'), may hold values from 0 to 31
- tile_count: int32 [32, 8], P('row', 'col'), may hold values from 32 to 128, as said below
Outputs:
- layer_out: bfloat16 [32, 8, 128, 512], P('row', 'col')
- weight_grad: float32 [512, 512], replicated
- feature_grad: bfloat16 [8, 32, 128, 512], P('col', 'row')
The draws below stay inside these ranges and needn't reach their ends.
Inputs may be any that keep to these rules, and one draw needn't show every extreme that they name: `tile_count`: live tile slots of each grid block; in every draw one block, drawn from the seed, has all 128 live. The (tile_rows, tile_cols) pairs of the 128 slots of one grid block are distinct.
All inputs are finite; a program needn't handle non-finite values.
Results may differ from the reference program's by a relative error of at most 0.005.
Values may be sent and summed in bfloat16 or wider, within the bound.
No kernel may reach another device: no remote copies, remote signals or barrier semaphores. Data moves between devices by JAX's collectives and lax.ppermute only.
A program may use at most 128 MiB of HBM per device.

```python
import math
import jax
import jax.numpy as jnp
from jax import lax

F = 512
TILE = 128
TR = 8
KMAX = 128
TC = 32
SUB = 128
N_ROW = 32
N_COL = 8


def tile_places(key):
    keys = jax.random.split(jax.random.fold_in(key, 7), N_ROW * N_COL)
    perms = jax.vmap(lambda k: jax.random.permutation(k, TR * TC)[:KMAX])(keys)
    perms = perms.reshape(N_ROW, N_COL, KMAX).astype(jnp.int32)
    return (perms // TC, perms % TC)


def draw_tile_rows(key, part):
    return tile_places(key)[0]


def draw_tile_cols(key, part):
    return tile_places(key)[1]


def draw_tile_count(key, part):
    lowest = max(1, KMAX // 4)
    counts = jax.random.randint(jax.random.fold_in(key, 3), (N_ROW * N_COL,), lowest, KMAX + 1)
    chosen = jax.random.randint(jax.random.fold_in(key, 5), (), 0, N_ROW * N_COL)
    counts = counts.at[chosen].set(KMAX)
    return counts.reshape(N_ROW, N_COL).astype(jnp.int32)


def block_levels(own_key, shape, shards, smallest, largest):
    def one(axis_at, blocks):
        draws = jax.random.uniform(jax.random.fold_in(jax.random.fold_in(own_key, 6), axis_at), (blocks,), jnp.float32, smallest / len(shards), largest / len(shards))
        return jnp.repeat(jnp.exp(draws), shape[axis_at] // blocks).reshape((-1,) + (1,) * (len(shape) - axis_at - 1))

    factor_of = one(*shards[0])
    for cut in shards[1:]:
        factor_of = factor_of * one(*cut)
    return factor_of


def bell_draw(own_key, shape, deviation, reach, shards=(), held_as=jnp.bfloat16):
    gain = block_levels(own_key, shape, shards, -0.22, 0.18) if shards else 1.0
    array = jax.random.normal(own_key, shape, jnp.float32) * deviation * gain
    return jnp.minimum(jnp.maximum(array, -reach), reach).astype(held_as)


def setup_inputs(seed: int = 0) -> dict:
    arg_keys = jax.random.split(jax.random.key(seed), 8)
    return {
        "features": bell_draw(arg_keys[0], (N_COL, N_ROW, SUB, F), 1.0, 6.0, ((0, 8), (1, 32))),
        "weight": bell_draw(arg_keys[1], (F, F), F ** -0.5, 0.25),
        "cotangent": bell_draw(arg_keys[2], (N_ROW, N_COL, SUB, F), 1.0, 6.0, ((0, 32), (1, 8))),
        "tile_vals": jnp.clip(1.0 * jax.random.uniform(arg_keys[3], (N_ROW, N_COL, KMAX, TILE, TILE), jnp.float32) ** block_levels(arg_keys[3], (N_ROW, N_COL, KMAX, TILE, TILE), ((0, 32), (1, 8)), -0.2, 0.2), 0.0, 1.0).astype(jnp.bfloat16),
        "tile_rows": draw_tile_rows(jax.random.fold_in(arg_keys[7], 71), 0),
        "tile_cols": draw_tile_cols(jax.random.fold_in(arg_keys[7], 71), 0),
        "tile_count": draw_tile_count(jax.random.fold_in(arg_keys[7], 71), 0),
    }


def reference(features, weight, cotangent, tile_vals, tile_rows, tile_cols, tile_count):
    nodes = N_ROW * TR * TILE
    total_slots = N_ROW * N_COL * KMAX
    group = math.gcd(total_slots, 256)
    x_tiles = features.reshape(nodes // TILE, TILE, F).astype(jnp.float32)
    live = (jnp.arange(KMAX, dtype=jnp.int32)[None, None, :] < tile_count[:, :, None]).astype(jnp.float32)
    glob_rows = (jnp.arange(N_ROW, dtype=jnp.int32)[:, None, None] * TR + tile_rows).reshape(-1, group)
    glob_cols = (jnp.arange(N_COL, dtype=jnp.int32)[None, :, None] * TC + tile_cols).reshape(-1, group)
    masks = live.reshape(-1, group)
    values = tile_vals.reshape(-1, group, TILE, TILE)

    def forward_step(carry, items):
        total, degsum = carry
        block, rid, cid, mask = items
        a = block.astype(jnp.float32) * mask[:, None, None]
        prod = jnp.einsum('gij,gjf->gif', a, x_tiles[cid])
        total = total.at[rid].add(prod)
        degsum = degsum.at[rid].add(lax.optimization_barrier(jnp.sum(a, axis=2)))
        return ((total, degsum), None)
    init = (jnp.zeros((nodes // TILE, TILE, F), jnp.float32), jnp.zeros((nodes // TILE, TILE), jnp.float32))
    (total, degsum), _ = lax.scan(forward_step, init, (values, glob_rows, glob_cols, masks))
    inv = lax.rsqrt(1.0 + degsum.reshape(nodes))
    aggregated = (inv[:, None] * total.reshape(nodes, F)).astype(jnp.bfloat16)
    layer_out = jnp.dot(aggregated, weight, preferred_element_type=jnp.float32).astype(jnp.bfloat16)
    grad_flat = cotangent.reshape(nodes, F)
    weight_grad = jnp.dot(aggregated.T, grad_flat, preferred_element_type=jnp.float32) * nodes ** (-0.5)
    scaled = (inv[:, None] * jnp.dot(grad_flat, weight.T, preferred_element_type=jnp.float32)).astype(jnp.bfloat16)
    s_tiles = scaled.reshape(nodes // TILE, TILE, F).astype(jnp.float32)

    def backward_step(back, items):
        block, rid, cid, mask = items
        a = block.astype(jnp.float32) * mask[:, None, None]
        prod = jnp.einsum('gji,gjf->gif', a, s_tiles[rid])
        return (back.at[cid].add(prod), None)
    back, _ = lax.scan(backward_step, jnp.zeros((nodes // TILE, TILE, F), jnp.float32), (values, glob_rows, glob_cols, masks))
    feature_grad = back.reshape(N_COL, N_ROW, SUB, F).astype(jnp.bfloat16)
    return (layer_out.reshape(N_ROW, N_COL, SUB, F), weight_grad, feature_grad)
```

```python
import jax
import jax.numpy as jnp
from jax import lax
from jax.sharding import PartitionSpec as P


def per_device(features, weight, cotangent, tile_vals, tile_rows, tile_cols, tile_count):
    sub_rows = features.shape[2]
    width = features.shape[3]
    slots = tile_vals.shape[2]
    tile = tile_vals.shape[3]
    rows_axis = lax.axis_size("row")
    cols_axis = lax.axis_size("col")
    tile_rows_blk = sub_rows * cols_axis // tile
    tile_cols_blk = sub_rows * rows_axis // tile
    places = tile_rows_blk * tile_cols_blk

    live = jnp.arange(slots, dtype=jnp.int32) < tile_count[0, 0]
    place = tile_rows[0, 0] * tile_cols_blk + tile_cols[0, 0]
    onehot = (place[:, None] == jnp.arange(places, dtype=jnp.int32)[None, :]) & live[:, None]
    onehot = onehot.astype(jnp.bfloat16).reshape(slots, tile_rows_blk, tile_cols_blk)
    dense = jnp.einsum(
        "kab,kij->aibj", onehot, tile_vals[0, 0], preferred_element_type=jnp.float32
    ).astype(jnp.bfloat16)

    local_deg = jnp.sum(dense.astype(jnp.float32), axis=(2, 3)).reshape(tile_rows_blk * tile)
    deg_own = lax.psum_scatter(local_deg, "col", scatter_dimension=0, tiled=True)
    inv_own = lax.rsqrt(1.0 + deg_own)

    grad_own = cotangent[0, 0]
    projected = lax.dot_general(
        grad_own, weight, (((1,), (1,)), ((), ())), preferred_element_type=jnp.float32
    )
    scaled_own = (inv_own[:, None] * projected).astype(jnp.bfloat16)
    scaled = lax.all_gather(scaled_own, "col", axis=0, tiled=True)
    scaled_tiles = scaled.reshape(tile_rows_blk, tile, width)
    back = jnp.einsum("aibj,aif->bjf", dense, scaled_tiles, preferred_element_type=jnp.float32)
    pieces = back.astype(jnp.bfloat16).reshape(rows_axis, sub_rows, width)
    arrived = lax.all_to_all(pieces, "row", 0, 0)
    ones = jnp.ones((rows_axis,), jnp.bfloat16)
    feature_grad = jnp.einsum(
        "r,rnf->nf", ones, arrived, preferred_element_type=jnp.float32
    ).astype(jnp.bfloat16)

    panel = lax.all_gather(features, "row", axis=1, tiled=True).reshape(tile_cols_blk, tile, width)
    total = jnp.einsum("aibj,bjf->aif", dense, panel, preferred_element_type=jnp.float32)
    partial_agg = total.reshape(tile_rows_blk * tile, width)
    summed = lax.psum_scatter(partial_agg, "col", scatter_dimension=0, tiled=True)
    aggregated = (inv_own[:, None] * summed).astype(jnp.bfloat16)
    layer_out = jnp.dot(aggregated, weight, preferred_element_type=jnp.float32).astype(jnp.bfloat16)
    nodes = sub_rows * rows_axis * cols_axis
    weight_term = lax.dot_general(
        aggregated, grad_own, (((0,), (0,)), ((), ())), preferred_element_type=jnp.float32
    )
    weight_pieces = weight_term.reshape(rows_axis, width // rows_axis, width)
    weight_part = jnp.sum(lax.all_to_all(weight_pieces, "row", 0, 0), axis=0)
    weight_part = lax.psum(weight_part, "col")
    weight_grad = lax.all_gather(weight_part, "row", axis=0, tiled=True) * nodes ** (-0.5)
    return (
        layer_out.reshape(1, 1, sub_rows, width),
        weight_grad,
        feature_grad.reshape(1, 1, sub_rows, width),
    )


def solution(mesh):
    return jax.shard_map(
        per_device,
        mesh=mesh,
        in_specs=(
            P("col", "row", None, None),
            P(),
            P("row", "col", None, None),
            P("row", "col", None, None, None),
            P("row", "col", None),
            P("row", "col", None),
            P("row", "col"),
        ),
        out_specs=(P("row", "col", None, None), P(), P("col", "row", None, None)),
        check_vma=False,
    )
```

```python
import jax
import jax.numpy as jnp
from jax import lax
from jax.sharding import PartitionSpec as P


def per_device(features, weight, cotangent, tile_vals, tile_rows, tile_cols, tile_count):
    sub_rows = features.shape[2]
    width = features.shape[3]
    slots = tile_vals.shape[2]
    tile = tile_vals.shape[3]
    rows_axis = lax.axis_size("row")
    cols_axis = lax.axis_size("col")
    tile_rows_blk = sub_rows * cols_axis // tile
    tile_cols_blk = sub_rows * rows_axis // tile
    places = tile_rows_blk * tile_cols_blk

    live = jnp.arange(slots, dtype=jnp.int32) < tile_count[0, 0]
    place = tile_rows[0, 0] * tile_cols_blk + tile_cols[0, 0]
    onehot = (place[:, None] == jnp.arange(places, dtype=jnp.int32)[None, :]) & live[:, None]
    onehot = onehot.astype(jnp.bfloat16).reshape(slots, tile_rows_blk, tile_cols_blk)
    dense = jnp.einsum(
        "kab,kij->aibj", onehot, tile_vals[0, 0], preferred_element_type=jnp.float32
    ).astype(jnp.bfloat16)

    local_deg = jnp.sum(dense.astype(jnp.float32), axis=(2, 3)).reshape(tile_rows_blk * tile)
    deg_all = lax.psum(local_deg, "col")
    inv_all = lax.rsqrt(1.0 + deg_all)
    me_col = lax.axis_index("col")
    inv_own = lax.dynamic_slice_in_dim(inv_all, me_col * sub_rows, sub_rows)

    grad_own = cotangent[0, 0]
    grad_rows = lax.all_gather(grad_own, "col", axis=0, tiled=True)
    projected = lax.dot_general(
        grad_rows, weight, (((1,), (1,)), ((), ())), preferred_element_type=jnp.float32
    )
    scaled = (inv_all[:, None] * projected).astype(jnp.bfloat16)
    scaled_tiles = scaled.reshape(tile_rows_blk, tile, width)
    back = jnp.einsum("aibj,aif->bjf", dense, scaled_tiles, preferred_element_type=jnp.float32)
    pieces = back.astype(jnp.bfloat16).reshape(rows_axis, sub_rows, width)
    arrived = lax.all_to_all(pieces, "row", 0, 0)
    ones = jnp.ones((rows_axis,), jnp.bfloat16)
    feature_grad = jnp.einsum(
        "r,rnf->nf", ones, arrived, preferred_element_type=jnp.float32
    ).astype(jnp.bfloat16)

    features, _ = lax.optimization_barrier((features, grad_rows))
    panel = lax.all_gather(features, "row", axis=1, tiled=True).reshape(tile_cols_blk, tile, width)
    panel, _ = lax.optimization_barrier((panel, arrived))
    total = jnp.einsum("aibj,bjf->aif", dense, panel, preferred_element_type=jnp.float32)
    partial_agg = total.reshape(tile_rows_blk * tile, width)
    summed = lax.psum_scatter(partial_agg, "col", scatter_dimension=0, tiled=True)
    aggregated = (inv_own[:, None] * summed).astype(jnp.bfloat16)
    layer_out = jnp.dot(aggregated, weight, preferred_element_type=jnp.float32).astype(jnp.bfloat16)
    nodes = sub_rows * rows_axis * cols_axis
    weight_term = lax.dot_general(
        aggregated, grad_own, (((0,), (0,)), ((), ())), preferred_element_type=jnp.float32
    )
    weight_pieces = weight_term.reshape(rows_axis, width // rows_axis, width)
    weight_part = jnp.sum(lax.all_to_all(weight_pieces, "row", 0, 0), axis=0)
    weight_pieces = weight_part.reshape(cols_axis, width // rows_axis // cols_axis, width)
    weight_part = jnp.sum(lax.all_to_all(weight_pieces, "col", 0, 0), axis=0) * nodes ** (-0.5)
    spread = jnp.broadcast_to(weight_part[None], (cols_axis,) + weight_part.shape)
    weight_part = lax.all_to_all(spread, "col", 0, 0).reshape(width // rows_axis, width)
    spread = jnp.broadcast_to(weight_part[None], (rows_axis,) + weight_part.shape)
    weight_grad = lax.all_to_all(spread, "row", 0, 0).reshape(width, width)
    return (
        layer_out.reshape(1, 1, sub_rows, width),
        weight_grad,
        feature_grad.reshape(1, 1, sub_rows, width),
    )


def solution(mesh):
    return jax.shard_map(
        per_device,
        mesh=mesh,
        in_specs=(
            P("col", "row", None, None),
            P(),
            P("row", "col", None, None),
            P("row", "col", None, None, None),
            P("row", "col", None),
            P("row", "col", None),
            P("row", "col"),
        ),
        out_specs=(P("row", "col", None, None), P(), P("col", "row", None, None)),
        check_vma=False,
    )
```

```python
import jax
import jax.numpy as jnp
from jax import lax
from jax.sharding import PartitionSpec as P


def per_device(features, weight, cotangent, tile_vals, tile_rows, tile_cols, tile_count):
    sub_rows = features.shape[2]
    width = features.shape[3]
    slots = tile_vals.shape[2]
    tile = tile_vals.shape[3]
    rows_axis = lax.axis_size("row")
    cols_axis = lax.axis_size("col")
    tile_rows_blk = sub_rows * cols_axis // tile
    tile_cols_blk = sub_rows * rows_axis // tile
    places = tile_rows_blk * tile_cols_blk

    live = jnp.arange(slots, dtype=jnp.int32) < tile_count[0, 0]
    place = tile_rows[0, 0] * tile_cols_blk + tile_cols[0, 0]
    onehot = (place[:, None] == jnp.arange(places, dtype=jnp.int32)[None, :]) & live[:, None]
    onehot = onehot.astype(jnp.bfloat16).reshape(slots, tile_rows_blk, tile_cols_blk)
    dense = jnp.einsum(
        "kab,kij->aibj", onehot, tile_vals[0, 0], preferred_element_type=jnp.float32
    ).astype(jnp.bfloat16)

    dense_t = jnp.einsum(
        "kab,kij->bjai", onehot, tile_vals[0, 0], preferred_element_type=jnp.float32
    ).astype(jnp.bfloat16)

    local_deg = jnp.sum(dense.astype(jnp.float32), axis=(2, 3)).reshape(tile_rows_blk * tile)
    deg_spread = jnp.broadcast_to(local_deg[None], (cols_axis,) + local_deg.shape)
    deg_all = jnp.sum(lax.all_to_all(deg_spread, "col", 0, 0), axis=0)
    inv_all = lax.rsqrt(1.0 + deg_all)
    me_col = lax.axis_index("col")
    inv_own = lax.dynamic_slice_in_dim(inv_all, me_col * sub_rows, sub_rows)

    grad_own = cotangent[0, 0]
    grad_rows = lax.all_gather(grad_own, "col", axis=0, tiled=True)
    projected = lax.dot_general(
        grad_rows, weight, (((1,), (1,)), ((), ())), preferred_element_type=jnp.float32
    )
    scaled = (inv_all[:, None] * projected).astype(jnp.bfloat16)
    scaled_tiles = scaled.reshape(tile_rows_blk, tile, width)
    back = jnp.einsum("bjai,aif->bjf", dense_t, scaled_tiles, preferred_element_type=jnp.float32)
    pieces = back.astype(jnp.bfloat16).reshape(rows_axis, sub_rows, width)
    arrived = lax.all_to_all(pieces, "row", 0, 0)
    ones = jnp.ones((rows_axis,), jnp.bfloat16)
    feature_grad = jnp.einsum(
        "r,rnf->nf", ones, arrived, preferred_element_type=jnp.float32
    ).astype(jnp.bfloat16)

    features, _ = lax.optimization_barrier((features, grad_rows))
    panel = lax.all_gather(features, "row", axis=1, tiled=True).reshape(tile_cols_blk, tile, width)
    panel, _ = lax.optimization_barrier((panel, arrived))
    total = jnp.einsum("aibj,bjf->aif", dense, panel, preferred_element_type=jnp.float32)
    partial_agg = total.reshape(tile_rows_blk * tile, width)
    scaled_partial = (inv_all[:, None] * partial_agg).astype(jnp.bfloat16)
    weight_term = lax.dot_general(
        scaled_partial, grad_rows, (((0,), (0,)), ((), ())), preferred_element_type=jnp.float32
    )
    summed = lax.psum_scatter(partial_agg, "col", scatter_dimension=0, tiled=True)
    aggregated = (inv_own[:, None] * summed).astype(jnp.bfloat16)
    layer_out = jnp.dot(aggregated, weight, preferred_element_type=jnp.float32).astype(jnp.bfloat16)
    nodes = sub_rows * rows_axis * cols_axis
    weight_pieces = weight_term.reshape(rows_axis, width // rows_axis, width)
    weight_part = jnp.sum(lax.all_to_all(weight_pieces, "row", 0, 0), axis=0)
    weight_pieces = weight_part.reshape(cols_axis, width // rows_axis // cols_axis, width)
    weight_part = jnp.sum(lax.all_to_all(weight_pieces, "col", 0, 0), axis=0) * nodes ** (-0.5)
    spread = jnp.broadcast_to(weight_part[None], (cols_axis,) + weight_part.shape)
    weight_part = lax.all_to_all(spread, "col", 0, 0).reshape(width // rows_axis, width)
    spread = jnp.broadcast_to(weight_part[None], (rows_axis,) + weight_part.shape)
    weight_grad = lax.all_to_all(spread, "row", 0, 0).reshape(width, width)
    return (
        layer_out.reshape(1, 1, sub_rows, width),
        weight_grad,
        feature_grad.reshape(1, 1, sub_rows, width),
    )


def solution(mesh):
    return jax.shard_map(
        per_device,
        mesh=mesh,
        in_specs=(
            P("col", "row", None, None),
            P(),
            P("row", "col", None, None),
            P("row", "col", None, None, None),
            P("row", "col", None),
            P("row", "col", None),
            P("row", "col"),
        ),
        out_specs=(P("row", "col", None, None), P(), P("col", "row", None, None)),
        check_vma=False,
    )
```

```python
import jax
import jax.numpy as jnp
from jax import lax
from jax.sharding import PartitionSpec as P


def per_device(features, weight, cotangent, tile_vals, tile_rows, tile_cols, tile_count):
    sub_rows = features.shape[2]
    width = features.shape[3]
    slots = tile_vals.shape[2]
    tile = tile_vals.shape[3]
    rows_axis = lax.axis_size("row")
    cols_axis = lax.axis_size("col")
    tile_rows_blk = sub_rows * cols_axis // tile
    tile_cols_blk = sub_rows * rows_axis // tile
    places = tile_rows_blk * tile_cols_blk

    live = jnp.arange(slots, dtype=jnp.int32) < tile_count[0, 0]
    place = tile_rows[0, 0] * tile_cols_blk + tile_cols[0, 0]
    onehot = (place[:, None] == jnp.arange(places, dtype=jnp.int32)[None, :]) & live[:, None]
    onehot = onehot.astype(jnp.bfloat16).reshape(slots, tile_rows_blk, tile_cols_blk)
    dense = jnp.einsum(
        "kab,kij->aibj", onehot, tile_vals[0, 0], preferred_element_type=jnp.float32
    ).astype(jnp.bfloat16)

    local_deg = jnp.sum(dense.astype(jnp.float32), axis=(2, 3)).reshape(tile_rows_blk * tile)
    deg_spread = jnp.broadcast_to(local_deg[None], (cols_axis,) + local_deg.shape)
    deg_all = jnp.sum(lax.all_to_all(deg_spread, "col", 0, 0), axis=0)
    inv_all = lax.rsqrt(1.0 + deg_all)
    me_col = lax.axis_index("col")
    inv_own = lax.dynamic_slice_in_dim(inv_all, me_col * sub_rows, sub_rows)

    grad_own = cotangent[0, 0]
    grad_rows = lax.all_gather(grad_own, "col", axis=0, tiled=True)
    projected = lax.dot_general(
        grad_rows, weight, (((1,), (1,)), ((), ())), preferred_element_type=jnp.float32
    )
    scaled = (inv_all[:, None] * projected).astype(jnp.bfloat16)
    dense_flat = dense.reshape(tile_rows_blk * tile, tile_cols_blk * tile)
    back_t = lax.dot_general(
        scaled, dense_flat, (((0,), (0,)), ((), ())), preferred_element_type=jnp.float32
    )
    pieces = back_t.astype(jnp.bfloat16).T.reshape(rows_axis, sub_rows, width)
    arrived = lax.all_to_all(pieces, "row", 0, 0)
    ones = jnp.ones((rows_axis,), jnp.bfloat16)
    feature_grad = jnp.einsum(
        "r,rnf->nf", ones, arrived, preferred_element_type=jnp.float32
    ).astype(jnp.bfloat16)

    features, _ = lax.optimization_barrier((features, grad_rows))
    panel = lax.all_gather(features, "row", axis=1, tiled=True).reshape(tile_cols_blk, tile, width)
    panel, _ = lax.optimization_barrier((panel, arrived))
    total = jnp.einsum("aibj,bjf->aif", dense, panel, preferred_element_type=jnp.float32)
    partial_agg = total.reshape(tile_rows_blk * tile, width)
    scaled_partial = (inv_all[:, None] * partial_agg).astype(jnp.bfloat16)
    weight_term = lax.dot_general(
        scaled_partial, grad_rows, (((0,), (0,)), ((), ())), preferred_element_type=jnp.float32
    )
    summed = lax.psum_scatter(partial_agg, "col", scatter_dimension=0, tiled=True)
    aggregated = (inv_own[:, None] * summed).astype(jnp.bfloat16)
    layer_out = jnp.dot(aggregated, weight, preferred_element_type=jnp.float32).astype(jnp.bfloat16)
    nodes = sub_rows * rows_axis * cols_axis
    weight_pieces = weight_term.reshape(cols_axis, width // cols_axis, width)
    weight_part = jnp.sum(lax.all_to_all(weight_pieces, "col", 0, 0), axis=0)
    weight_pieces = weight_part.reshape(rows_axis, width // cols_axis // rows_axis, width)
    weight_part = jnp.sum(lax.all_to_all(weight_pieces, "row", 0, 0), axis=0) * nodes ** (-0.5)
    spread = jnp.broadcast_to(weight_part[None], (rows_axis,) + weight_part.shape)
    weight_part = lax.all_to_all(spread, "row", 0, 0).reshape(width // cols_axis, width)
    spread = jnp.broadcast_to(weight_part[None], (cols_axis,) + weight_part.shape)
    weight_grad = lax.all_to_all(spread, "col", 0, 0).reshape(width, width)
    return (
        layer_out.reshape(1, 1, sub_rows, width),
        weight_grad,
        feature_grad.reshape(1, 1, sub_rows, width),
    )


def solution(mesh):
    return jax.shard_map(
        per_device,
        mesh=mesh,
        in_specs=(
            P("col", "row", None, None),
            P(),
            P("row", "col", None, None),
            P("row", "col", None, None, None),
            P("row", "col", None),
            P("row", "col", None),
            P("row", "col"),
        ),
        out_specs=(P("row", "col", None, None), P(), P("col", "row", None, None)),
        check_vma=False,
    )
```

```python
import jax
import jax.numpy as jnp
from jax import lax
from jax.sharding import PartitionSpec as P


def per_device(features, weight, cotangent, tile_vals, tile_rows, tile_cols, tile_count):
    sub_rows = features.shape[2]
    width = features.shape[3]
    slots = tile_vals.shape[2]
    tile = tile_vals.shape[3]
    rows_axis = lax.axis_size("row")
    cols_axis = lax.axis_size("col")
    tile_rows_blk = sub_rows * cols_axis // tile
    tile_cols_blk = sub_rows * rows_axis // tile
    places = tile_rows_blk * tile_cols_blk

    live = jnp.arange(slots, dtype=jnp.int32) < tile_count[0, 0]
    place = tile_rows[0, 0] * tile_cols_blk + tile_cols[0, 0]
    onehot = (place[:, None] == jnp.arange(places, dtype=jnp.int32)[None, :]) & live[:, None]
    onehot = onehot.astype(jnp.bfloat16).reshape(slots, tile_rows_blk, tile_cols_blk)
    dense = jnp.einsum(
        "kab,kij->aibj", onehot, tile_vals[0, 0], preferred_element_type=jnp.float32
    ).astype(jnp.bfloat16)

    local_deg = jnp.sum(dense.astype(jnp.float32), axis=(2, 3)).reshape(tile_rows_blk * tile)
    deg_spread = jnp.broadcast_to(local_deg[None], (cols_axis,) + local_deg.shape)
    deg_all = jnp.sum(lax.all_to_all(deg_spread, "col", 0, 0), axis=0)
    inv_all = lax.rsqrt(1.0 + deg_all)
    me_col = lax.axis_index("col")
    inv_own = lax.dynamic_slice_in_dim(inv_all, me_col * sub_rows, sub_rows)

    grad_own = cotangent[0, 0]
    grad_spread = jnp.broadcast_to(grad_own[None], (cols_axis,) + grad_own.shape)
    grad_rows = lax.all_to_all(grad_spread, "col", 0, 0).reshape(cols_axis * sub_rows, width)
    projected = lax.dot_general(
        grad_rows, weight, (((1,), (1,)), ((), ())), preferred_element_type=jnp.float32
    )
    scaled = (inv_all[:, None] * projected).astype(jnp.bfloat16)
    dense_flat = dense.reshape(tile_rows_blk * tile, tile_cols_blk * tile)
    back_t = lax.dot_general(
        scaled, dense_flat, (((0,), (0,)), ((), ())), preferred_element_type=jnp.float32
    )
    pieces = back_t.astype(jnp.bfloat16).T.reshape(rows_axis, sub_rows, width)
    arrived = lax.all_to_all(pieces, "row", 0, 0)
    ones = jnp.ones((rows_axis,), jnp.bfloat16)
    feature_grad = jnp.einsum(
        "r,rnf->nf", ones, arrived, preferred_element_type=jnp.float32
    ).astype(jnp.bfloat16)

    panel = lax.all_gather(features, "row", axis=1, tiled=True).reshape(tile_cols_blk, tile, width)
    panel, _ = lax.optimization_barrier((panel, pieces))
    total = jnp.einsum("aibj,bjf->aif", dense, panel, preferred_element_type=jnp.float32)
    partial_agg = total.reshape(tile_rows_blk * tile, width)
    scaled_partial = (inv_all[:, None] * partial_agg).astype(jnp.bfloat16)
    weight_term = lax.dot_general(
        scaled_partial, grad_rows, (((0,), (0,)), ((), ())), preferred_element_type=jnp.float32
    )
    weight_term, _ = lax.optimization_barrier((weight_term, arrived))
    summed = lax.psum_scatter(partial_agg, "col", scatter_dimension=0, tiled=True)
    aggregated = (inv_own[:, None] * summed).astype(jnp.bfloat16)
    layer_out = jnp.dot(aggregated, weight, preferred_element_type=jnp.float32).astype(jnp.bfloat16)
    nodes = sub_rows * rows_axis * cols_axis
    weight_pieces = weight_term.reshape(cols_axis, width // cols_axis, width)
    weight_part = jnp.sum(lax.all_to_all(weight_pieces, "col", 0, 0), axis=0)
    weight_pieces = weight_part.reshape(rows_axis, width // cols_axis // rows_axis, width)
    weight_part = jnp.sum(lax.all_to_all(weight_pieces, "row", 0, 0), axis=0) * nodes ** (-0.5)
    spread = jnp.broadcast_to(weight_part[None], (rows_axis,) + weight_part.shape)
    weight_part = lax.all_to_all(spread, "row", 0, 0).reshape(width // cols_axis, width)
    spread = jnp.broadcast_to(weight_part[None], (cols_axis,) + weight_part.shape)
    weight_grad = lax.all_to_all(spread, "col", 0, 0).reshape(width, width)
    return (
        layer_out.reshape(1, 1, sub_rows, width),
        weight_grad,
        feature_grad.reshape(1, 1, sub_rows, width),
    )


def solution(mesh):
    return jax.shard_map(
        per_device,
        mesh=mesh,
        in_specs=(
            P("col", "row", None, None),
            P(),
            P("row", "col", None, None),
            P("row", "col", None, None, None),
            P("row", "col", None),
            P("row", "col", None),
            P("row", "col"),
        ),
        out_specs=(P("row", "col", None, None), P(), P("col", "row", None, None)),
        check_vma=False,
    )
```

```python
import jax
import jax.numpy as jnp
from jax import lax
from jax.sharding import PartitionSpec as P


def per_device(features, weight, cotangent, tile_vals, tile_rows, tile_cols, tile_count):
    sub_rows = features.shape[2]
    width = features.shape[3]
    slots = tile_vals.shape[2]
    tile = tile_vals.shape[3]
    rows_axis = lax.axis_size("row")
    cols_axis = lax.axis_size("col")
    tile_rows_blk = sub_rows * cols_axis // tile
    tile_cols_blk = sub_rows * rows_axis // tile
    places = tile_rows_blk * tile_cols_blk

    live = jnp.arange(slots, dtype=jnp.int32) < tile_count[0, 0]
    place = tile_rows[0, 0] * tile_cols_blk + tile_cols[0, 0]
    onehot = (place[:, None] == jnp.arange(places, dtype=jnp.int32)[None, :]) & live[:, None]
    onehot = onehot.astype(jnp.bfloat16).reshape(slots, tile_rows_blk, tile_cols_blk)
    dense = jnp.einsum(
        "kab,kij->aibj", onehot, tile_vals[0, 0], preferred_element_type=jnp.float32
    ).astype(jnp.bfloat16)

    local_deg = jnp.sum(dense.astype(jnp.float32), axis=(2, 3)).reshape(tile_rows_blk * tile)
    deg_spread = jnp.broadcast_to(local_deg[None], (cols_axis,) + local_deg.shape)
    deg_all = jnp.sum(lax.all_to_all(deg_spread, "col", 0, 0), axis=0)
    inv_all = lax.rsqrt(1.0 + deg_all)
    me_col = lax.axis_index("col")
    inv_own = lax.dynamic_slice_in_dim(inv_all, me_col * sub_rows, sub_rows)

    grad_own = cotangent[0, 0]
    grad_spread = jnp.broadcast_to(grad_own[None], (cols_axis,) + grad_own.shape)
    grad_rows = lax.all_to_all(grad_spread, "col", 0, 0).reshape(cols_axis * sub_rows, width)
    projected = lax.dot_general(
        grad_rows, weight, (((1,), (1,)), ((), ())), preferred_element_type=jnp.float32
    )
    scaled = (inv_all[:, None] * projected).astype(jnp.bfloat16)
    dense_flat = dense.reshape(tile_rows_blk * tile, tile_cols_blk * tile)
    back_t = lax.dot_general(
        scaled, dense_flat, (((0,), (0,)), ((), ())), preferred_element_type=jnp.float32
    )
    half = width // 2
    odd = lax.axis_index("row") % 2 == 1
    low, high = back_t[:half], back_t[half:]
    keep = jnp.where(odd, high, low)
    give = jnp.where(odd, low, high)
    partner = [(i, i ^ 1) for i in range(rows_axis)]
    chip_sum = keep + lax.ppermute(give, "row", partner)
    pieces = chip_sum.astype(jnp.bfloat16).T.reshape(rows_axis, sub_rows, half)
    arrived = lax.all_to_all(pieces, "row", 0, 0)
    parity = jnp.arange(rows_axis, dtype=jnp.int32) % 2
    from_even = (parity == 0).astype(jnp.bfloat16)
    from_odd = (parity == 1).astype(jnp.bfloat16)
    grad_low = jnp.einsum("r,rnf->nf", from_even, arrived, preferred_element_type=jnp.float32)
    grad_high = jnp.einsum("r,rnf->nf", from_odd, arrived, preferred_element_type=jnp.float32)
    feature_grad = jnp.concatenate([grad_low, grad_high], axis=1).astype(jnp.bfloat16)

    panel = lax.all_gather(features, "row", axis=1, tiled=True).reshape(tile_cols_blk, tile, width)
    panel, _ = lax.optimization_barrier((panel, pieces))
    total = jnp.einsum("aibj,bjf->aif", dense, panel, preferred_element_type=jnp.float32)
    partial_agg = total.reshape(tile_rows_blk * tile, width)
    scaled_partial = (inv_all[:, None] * partial_agg).astype(jnp.bfloat16)
    weight_term = lax.dot_general(
        scaled_partial, grad_rows, (((0,), (0,)), ((), ())), preferred_element_type=jnp.float32
    )
    weight_term, _ = lax.optimization_barrier((weight_term, arrived))
    summed = lax.psum_scatter(partial_agg, "col", scatter_dimension=0, tiled=True)
    aggregated = (inv_own[:, None] * summed).astype(jnp.bfloat16)
    layer_out = jnp.dot(aggregated, weight, preferred_element_type=jnp.float32).astype(jnp.bfloat16)
    nodes = sub_rows * rows_axis * cols_axis
    weight_pieces = weight_term.reshape(cols_axis, width // cols_axis, width)
    weight_part = jnp.sum(lax.all_to_all(weight_pieces, "col", 0, 0), axis=0)
    weight_pieces = weight_part.reshape(rows_axis, width // cols_axis // rows_axis, width)
    weight_part = jnp.sum(lax.all_to_all(weight_pieces, "row", 0, 0), axis=0) * nodes ** (-0.5)
    spread = jnp.broadcast_to(weight_part[None], (rows_axis,) + weight_part.shape)
    weight_part = lax.all_to_all(spread, "row", 0, 0).reshape(width // cols_axis, width)
    spread = jnp.broadcast_to(weight_part[None], (cols_axis,) + weight_part.shape)
    weight_grad = lax.all_to_all(spread, "col", 0, 0).reshape(width, width)
    return (
        layer_out.reshape(1, 1, sub_rows, width),
        weight_grad,
        feature_grad.reshape(1, 1, sub_rows, width),
    )


def solution(mesh):
    return jax.shard_map(
        per_device,
        mesh=mesh,
        in_specs=(
            P("col", "row", None, None),
            P(),
            P("row", "col", None, None),
            P("row", "col", None, None, None),
            P("row", "col", None),
            P("row", "col", None),
            P("row", "col"),
        ),
        out_specs=(P("row", "col", None, None), P(), P("col", "row", None, None)),
        check_vma=False,
    )
```

```python
import jax
import jax.numpy as jnp
from jax import lax
from jax.sharding import PartitionSpec as P


def per_device(features, weight, cotangent, tile_vals, tile_rows, tile_cols, tile_count):
    sub_rows = features.shape[2]
    width = features.shape[3]
    slots = tile_vals.shape[2]
    tile = tile_vals.shape[3]
    rows_axis = lax.axis_size("row")
    cols_axis = lax.axis_size("col")
    tile_rows_blk = sub_rows * cols_axis // tile
    tile_cols_blk = sub_rows * rows_axis // tile
    places = tile_rows_blk * tile_cols_blk

    live = jnp.arange(slots, dtype=jnp.int32) < tile_count[0, 0]
    place = tile_rows[0, 0] * tile_cols_blk + tile_cols[0, 0]
    onehot = (place[:, None] == jnp.arange(places, dtype=jnp.int32)[None, :]) & live[:, None]
    onehot = onehot.astype(jnp.bfloat16).reshape(slots, tile_rows_blk, tile_cols_blk)
    dense = jnp.einsum(
        "kab,kij->aibj", onehot, tile_vals[0, 0], preferred_element_type=jnp.float32
    ).astype(jnp.bfloat16)

    local_deg = jnp.sum(dense.astype(jnp.float32), axis=(2, 3)).reshape(tile_rows_blk * tile)
    grad_own = cotangent[0, 0]
    deg_round = lax.reduce_precision(local_deg, exponent_bits=8, mantissa_bits=7)
    deg_high = deg_round.astype(jnp.bfloat16)
    deg_low = (local_deg - deg_round).astype(jnp.bfloat16)
    extra = jnp.zeros((16, width), jnp.bfloat16)
    extra = extra.at[0:2].set(deg_high.reshape(2, width)).at[2:4].set(deg_low.reshape(2, width))
    payload = jnp.concatenate([grad_own, extra], axis=0)
    spread = jnp.broadcast_to(payload[None], (cols_axis,) + payload.shape)
    got = lax.all_to_all(spread, "col", 0, 0)
    grad_rows = got[:, :sub_rows].reshape(cols_axis * sub_rows, width)
    deg_parts = got[:, sub_rows:sub_rows + 4].astype(jnp.float32)
    deg_all = jnp.sum(deg_parts[:, 0:2] + deg_parts[:, 2:4], axis=0).reshape(-1)
    inv_all = lax.rsqrt(1.0 + deg_all)
    me_col = lax.axis_index("col")
    inv_own = lax.dynamic_slice_in_dim(inv_all, me_col * sub_rows, sub_rows)

    projected = lax.dot_general(
        grad_rows, weight, (((1,), (1,)), ((), ())), preferred_element_type=jnp.float32
    )
    scaled = (inv_all[:, None] * projected).astype(jnp.bfloat16)
    dense_flat = dense.reshape(tile_rows_blk * tile, tile_cols_blk * tile)
    back_t = lax.dot_general(
        scaled, dense_flat, (((0,), (0,)), ((), ())), preferred_element_type=jnp.float32
    )
    half = width // 2
    odd = lax.axis_index("row") % 2 == 1
    low, high = back_t[:half], back_t[half:]
    keep = jnp.where(odd, high, low)
    give = jnp.where(odd, low, high)
    partner = [(i, i ^ 1) for i in range(rows_axis)]
    chip_sum = keep + lax.ppermute(give, "row", partner)
    pieces = chip_sum.astype(jnp.bfloat16).T.reshape(rows_axis, sub_rows, half)
    arrived = lax.all_to_all(pieces, "row", 0, 0)
    parity = jnp.arange(rows_axis, dtype=jnp.int32) % 2
    from_even = (parity == 0).astype(jnp.bfloat16)
    from_odd = (parity == 1).astype(jnp.bfloat16)
    grad_low = jnp.einsum("r,rnf->nf", from_even, arrived, preferred_element_type=jnp.float32)
    grad_high = jnp.einsum("r,rnf->nf", from_odd, arrived, preferred_element_type=jnp.float32)
    feature_grad = jnp.concatenate([grad_low, grad_high], axis=1).astype(jnp.bfloat16)

    panel = lax.all_gather(features, "row", axis=1, tiled=True).reshape(tile_cols_blk, tile, width)
    panel, _ = lax.optimization_barrier((panel, pieces))
    total = jnp.einsum("aibj,bjf->aif", dense, panel, preferred_element_type=jnp.float32)
    partial_agg = total.reshape(tile_rows_blk * tile, width)
    scaled_partial = (inv_all[:, None] * partial_agg).astype(jnp.bfloat16)
    weight_term = lax.dot_general(
        scaled_partial, grad_rows, (((0,), (0,)), ((), ())), preferred_element_type=jnp.float32
    )
    weight_term, _ = lax.optimization_barrier((weight_term, arrived))
    summed = lax.psum_scatter(partial_agg, "col", scatter_dimension=0, tiled=True)
    aggregated = (inv_own[:, None] * summed).astype(jnp.bfloat16)
    layer_out = jnp.dot(aggregated, weight, preferred_element_type=jnp.float32).astype(jnp.bfloat16)
    nodes = sub_rows * rows_axis * cols_axis
    weight_pieces = weight_term.astype(jnp.bfloat16).reshape(cols_axis, width // cols_axis, width)
    ones_col = jnp.ones((cols_axis,), jnp.bfloat16)
    weight_part = jnp.einsum(
        "c,cnf->nf", ones_col, lax.all_to_all(weight_pieces, "col", 0, 0),
        preferred_element_type=jnp.float32,
    )
    weight_pieces = weight_part.reshape(rows_axis, width // cols_axis // rows_axis, width)
    weight_part = jnp.sum(lax.all_to_all(weight_pieces, "row", 0, 0), axis=0) * nodes ** (-0.5)
    spread = jnp.broadcast_to(weight_part[None], (rows_axis,) + weight_part.shape)
    weight_part = lax.all_to_all(spread, "row", 0, 0).reshape(width // cols_axis, width)
    spread = jnp.broadcast_to(weight_part[None], (cols_axis,) + weight_part.shape)
    weight_grad = lax.all_to_all(spread, "col", 0, 0).reshape(width, width)
    return (
        layer_out.reshape(1, 1, sub_rows, width),
        weight_grad,
        feature_grad.reshape(1, 1, sub_rows, width),
    )


def solution(mesh):
    return jax.shard_map(
        per_device,
        mesh=mesh,
        in_specs=(
            P("col", "row", None, None),
            P(),
            P("row", "col", None, None),
            P("row", "col", None, None, None),
            P("row", "col", None),
            P("row", "col", None),
            P("row", "col"),
        ),
        out_specs=(P("row", "col", None, None), P(), P("col", "row", None, None)),
        check_vma=False,
    )
```

```python
import jax
import jax.numpy as jnp
from jax import lax
from jax.sharding import PartitionSpec as P


def per_device(features, weight, cotangent, tile_vals, tile_rows, tile_cols, tile_count):
    sub_rows = features.shape[2]
    width = features.shape[3]
    slots = tile_vals.shape[2]
    tile = tile_vals.shape[3]
    rows_axis = lax.axis_size("row")
    cols_axis = lax.axis_size("col")
    tile_rows_blk = sub_rows * cols_axis // tile
    tile_cols_blk = sub_rows * rows_axis // tile
    places = tile_rows_blk * tile_cols_blk

    live = jnp.arange(slots, dtype=jnp.int32) < tile_count[0, 0]
    place = tile_rows[0, 0] * tile_cols_blk + tile_cols[0, 0]
    onehot = (place[:, None] == jnp.arange(places, dtype=jnp.int32)[None, :]) & live[:, None]
    onehot = onehot.astype(jnp.bfloat16).reshape(slots, tile_rows_blk, tile_cols_blk)
    dense = jnp.einsum(
        "kab,kij->aibj", onehot, tile_vals[0, 0], preferred_element_type=jnp.float32
    ).astype(jnp.bfloat16)

    local_deg = jnp.sum(dense.astype(jnp.float32), axis=(2, 3)).reshape(tile_rows_blk * tile)
    grad_own = cotangent[0, 0]
    deg_round = lax.reduce_precision(local_deg, exponent_bits=8, mantissa_bits=7)
    deg_high = deg_round.astype(jnp.bfloat16)
    deg_low = (local_deg - deg_round).astype(jnp.bfloat16)
    extra = jnp.zeros((16, width), jnp.bfloat16)
    extra = extra.at[0:2].set(deg_high.reshape(2, width)).at[2:4].set(deg_low.reshape(2, width))
    payload = jnp.concatenate([grad_own, extra], axis=0)
    spread = jnp.broadcast_to(payload[None], (cols_axis,) + payload.shape)
    got = lax.all_to_all(spread, "col", 0, 0)
    grad_rows = got[:, :sub_rows].reshape(cols_axis * sub_rows, width)
    deg_parts = got[:, sub_rows:sub_rows + 4].astype(jnp.float32)
    deg_all = jnp.sum(deg_parts[:, 0:2] + deg_parts[:, 2:4], axis=0).reshape(-1)
    inv_all = lax.rsqrt(1.0 + deg_all)
    me_col = lax.axis_index("col")
    inv_own = lax.dynamic_slice_in_dim(inv_all, me_col * sub_rows, sub_rows)

    projected = lax.dot_general(
        grad_rows, weight, (((1,), (1,)), ((), ())), preferred_element_type=jnp.float32
    )
    scaled = (inv_all[:, None] * projected).astype(jnp.bfloat16)
    dense_flat = dense.reshape(tile_rows_blk * tile, tile_cols_blk * tile)
    back_t = lax.dot_general(
        scaled, dense_flat, (((0,), (0,)), ((), ())), preferred_element_type=jnp.float32
    )
    half = width // 2
    odd = lax.axis_index("row") % 2 == 1
    low, high = back_t[:half], back_t[half:]
    keep = jnp.where(odd, high, low)
    give = jnp.where(odd, low, high)
    partner = [(i, i ^ 1) for i in range(rows_axis)]
    chip_sum = keep + lax.ppermute(give, "row", partner)
    pieces = chip_sum.astype(jnp.bfloat16).T.reshape(rows_axis, sub_rows, half)
    arrived = lax.all_to_all(pieces, "row", 0, 0)
    parity = jnp.arange(rows_axis, dtype=jnp.int32) % 2
    from_even = (parity == 0).astype(jnp.bfloat16)
    from_odd = (parity == 1).astype(jnp.bfloat16)
    grad_low = jnp.einsum("r,rnf->nf", from_even, arrived, preferred_element_type=jnp.float32)
    grad_high = jnp.einsum("r,rnf->nf", from_odd, arrived, preferred_element_type=jnp.float32)
    feature_grad = jnp.concatenate([grad_low, grad_high], axis=1).astype(jnp.bfloat16)

    panel = lax.all_gather(features, "row", axis=1, tiled=True).reshape(tile_cols_blk, tile, width)
    panel, _ = lax.optimization_barrier((panel, pieces))
    total = jnp.einsum("aibj,bjf->aif", dense, panel, preferred_element_type=jnp.float32)
    partial_agg = total.reshape(tile_rows_blk * tile, width)
    scaled_partial = (inv_all[:, None] * partial_agg).astype(jnp.bfloat16)
    weight_term = lax.dot_general(
        scaled_partial, grad_rows, (((0,), (0,)), ((), ())), preferred_element_type=jnp.float32
    )
    summed = lax.psum_scatter(partial_agg, "col", scatter_dimension=0, tiled=True)
    aggregated = (inv_own[:, None] * summed).astype(jnp.bfloat16)
    layer_out = jnp.dot(aggregated, weight, preferred_element_type=jnp.float32).astype(jnp.bfloat16)
    nodes = sub_rows * rows_axis * cols_axis
    me_col = lax.axis_index("col")
    weight_part = weight_term
    step = cols_axis // 2
    while step >= 1:
        rows_now = weight_part.shape[0] // 2
        upper = (me_col // step) % 2 == 1
        keep = jnp.where(upper, weight_part[rows_now:], weight_part[:rows_now])
        give = jnp.where(upper, weight_part[:rows_now], weight_part[rows_now:])
        pairs = [(i, i ^ step) for i in range(cols_axis)]
        weight_part = keep + lax.ppermute(give, "col", pairs)
        step //= 2
    weight_part, _ = lax.optimization_barrier((weight_part, arrived))
    weight_pieces = weight_part.reshape(rows_axis, width // cols_axis // rows_axis, width)
    weight_part = jnp.sum(lax.all_to_all(weight_pieces, "row", 0, 0), axis=0) * nodes ** (-0.5)
    spread = jnp.broadcast_to(weight_part[None], (rows_axis,) + weight_part.shape)
    weight_part = lax.all_to_all(spread, "row", 0, 0).reshape(width // cols_axis, width)
    spread = jnp.broadcast_to(weight_part[None], (cols_axis,) + weight_part.shape)
    weight_grad = lax.all_to_all(spread, "col", 0, 0).reshape(width, width)
    return (
        layer_out.reshape(1, 1, sub_rows, width),
        weight_grad,
        feature_grad.reshape(1, 1, sub_rows, width),
    )


def solution(mesh):
    return jax.shard_map(
        per_device,
        mesh=mesh,
        in_specs=(
            P("col", "row", None, None),
            P(),
            P("row", "col", None, None),
            P("row", "col", None, None, None),
            P("row", "col", None),
            P("row", "col", None),
            P("row", "col"),
        ),
        out_specs=(P("row", "col", None, None), P(), P("col", "row", None, None)),
        check_vma=False,
    )
```

```python
import jax
import jax.numpy as jnp
from jax import lax
from jax.sharding import PartitionSpec as P


def per_device(features, weight, cotangent, tile_vals, tile_rows, tile_cols, tile_count):
    sub_rows = features.shape[2]
    width = features.shape[3]
    slots = tile_vals.shape[2]
    tile = tile_vals.shape[3]
    rows_axis = lax.axis_size("row")
    cols_axis = lax.axis_size("col")
    tile_rows_blk = sub_rows * cols_axis // tile
    tile_cols_blk = sub_rows * rows_axis // tile
    places = tile_rows_blk * tile_cols_blk

    live = jnp.arange(slots, dtype=jnp.int32) < tile_count[0, 0]
    place = tile_rows[0, 0] * tile_cols_blk + tile_cols[0, 0]
    onehot = (place[:, None] == jnp.arange(places, dtype=jnp.int32)[None, :]) & live[:, None]
    onehot = onehot.astype(jnp.bfloat16).reshape(slots, tile_rows_blk, tile_cols_blk)
    dense = jnp.einsum(
        "kab,kij->aibj", onehot, tile_vals[0, 0], preferred_element_type=jnp.float32
    ).astype(jnp.bfloat16)

    local_deg = jnp.sum(dense.astype(jnp.float32), axis=(2, 3)).reshape(tile_rows_blk * tile)
    grad_own = cotangent[0, 0]
    deg_round = lax.reduce_precision(local_deg, exponent_bits=8, mantissa_bits=7)
    deg_high = deg_round.astype(jnp.bfloat16)
    deg_low = (local_deg - deg_round).astype(jnp.bfloat16)
    extra = jnp.zeros((16, width), jnp.bfloat16)
    extra = extra.at[0:2].set(deg_high.reshape(2, width)).at[2:4].set(deg_low.reshape(2, width))
    payload = jnp.concatenate([grad_own, extra], axis=0)
    spread = jnp.broadcast_to(payload[None], (cols_axis,) + payload.shape)
    got = lax.all_to_all(spread, "col", 0, 0)
    grad_rows = got[:, :sub_rows].reshape(cols_axis * sub_rows, width)
    deg_parts = got[:, sub_rows:sub_rows + 4].astype(jnp.float32)
    deg_all = jnp.sum(deg_parts[:, 0:2] + deg_parts[:, 2:4], axis=0).reshape(-1)
    inv_all = lax.rsqrt(1.0 + deg_all)
    me_col = lax.axis_index("col")
    inv_own = lax.dynamic_slice_in_dim(inv_all, me_col * sub_rows, sub_rows)

    projected = lax.dot_general(
        grad_rows, weight, (((1,), (1,)), ((), ())), preferred_element_type=jnp.float32
    )
    scaled = (inv_all[:, None] * projected).astype(jnp.bfloat16)
    dense_flat = dense.reshape(tile_rows_blk * tile, tile_cols_blk * tile)
    back_t = lax.dot_general(
        scaled, dense_flat, (((0,), (0,)), ((), ())), preferred_element_type=jnp.float32
    )
    half = width // 2
    odd = lax.axis_index("row") % 2 == 1
    low, high = back_t[:half], back_t[half:]
    keep = jnp.where(odd, high, low)
    give = jnp.where(odd, low, high)
    partner = [(i, i ^ 1) for i in range(rows_axis)]
    chip_sum = keep + lax.ppermute(give, "row", partner)
    pieces = chip_sum.astype(jnp.bfloat16).T.reshape(rows_axis, sub_rows, half)
    arrived = lax.all_to_all(pieces, "row", 0, 0)
    parity = jnp.arange(rows_axis, dtype=jnp.int32) % 2
    from_even = (parity == 0).astype(jnp.bfloat16)
    from_odd = (parity == 1).astype(jnp.bfloat16)
    grad_low = jnp.einsum("r,rnf->nf", from_even, arrived, preferred_element_type=jnp.float32)
    grad_high = jnp.einsum("r,rnf->nf", from_odd, arrived, preferred_element_type=jnp.float32)
    feature_grad = jnp.concatenate([grad_low, grad_high], axis=1).astype(jnp.bfloat16)

    panel = lax.all_gather(features, "row", axis=1, tiled=True).reshape(tile_cols_blk, tile, width)
    panel, _ = lax.optimization_barrier((panel, pieces))
    total = jnp.einsum("aibj,bjf->aif", dense, panel, preferred_element_type=jnp.float32)
    partial_agg = total.reshape(tile_rows_blk * tile, width)
    scaled_partial = (inv_all[:, None] * partial_agg).astype(jnp.bfloat16)
    weight_term = lax.dot_general(
        scaled_partial, grad_rows, (((0,), (0,)), ((), ())), preferred_element_type=jnp.float32
    )
    weight_term, _ = lax.optimization_barrier((weight_term, arrived))
    summed = lax.psum_scatter(partial_agg, "col", scatter_dimension=0, tiled=True)
    aggregated = (inv_own[:, None] * summed).astype(jnp.bfloat16)
    layer_out = jnp.dot(aggregated, weight, preferred_element_type=jnp.float32).astype(jnp.bfloat16)
    nodes = sub_rows * rows_axis * cols_axis
    weight_pieces = weight_term.astype(jnp.bfloat16).reshape(cols_axis, width // cols_axis, width)
    ones_col = jnp.ones((cols_axis,), jnp.bfloat16)
    weight_part = jnp.einsum(
        "c,cnf->nf", ones_col, lax.all_to_all(weight_pieces, "col", 0, 0),
        preferred_element_type=jnp.float32,
    )
    weight_pieces = weight_part.reshape(rows_axis, width // cols_axis // rows_axis, width)
    weight_part = jnp.sum(lax.all_to_all(weight_pieces, "row", 0, 0), axis=0) * nodes ** (-0.5)
    spread = jnp.broadcast_to(weight_part[None], (cols_axis * rows_axis,) + weight_part.shape)
    weight_grad = lax.all_to_all(spread, ("col", "row"), 0, 0).reshape(width, width)
    return (
        layer_out.reshape(1, 1, sub_rows, width),
        weight_grad,
        feature_grad.reshape(1, 1, sub_rows, width),
    )


def solution(mesh):
    return jax.shard_map(
        per_device,
        mesh=mesh,
        in_specs=(
            P("col", "row", None, None),
            P(),
            P("row", "col", None, None),
            P("row", "col", None, None, None),
            P("row", "col", None),
            P("row", "col", None),
            P("row", "col"),
        ),
        out_specs=(P("row", "col", None, None), P(), P("col", "row", None, None)),
        check_vma=False,
    )
```

```python
import jax
import jax.numpy as jnp
from jax import lax
from jax.sharding import PartitionSpec as P


def per_device(features, weight, cotangent, tile_vals, tile_rows, tile_cols, tile_count):
    sub_rows = features.shape[2]
    width = features.shape[3]
    slots = tile_vals.shape[2]
    tile = tile_vals.shape[3]
    rows_axis = lax.axis_size("row")
    cols_axis = lax.axis_size("col")
    tile_rows_blk = sub_rows * cols_axis // tile
    tile_cols_blk = sub_rows * rows_axis // tile
    places = tile_rows_blk * tile_cols_blk

    live = jnp.arange(slots, dtype=jnp.int32) < tile_count[0, 0]
    place = tile_rows[0, 0] * tile_cols_blk + tile_cols[0, 0]
    onehot = (place[:, None] == jnp.arange(places, dtype=jnp.int32)[None, :]) & live[:, None]
    onehot = onehot.astype(jnp.bfloat16).reshape(slots, tile_rows_blk, tile_cols_blk)
    dense = jnp.einsum(
        "kab,kij->aibj", onehot, tile_vals[0, 0], preferred_element_type=jnp.float32
    ).astype(jnp.bfloat16)

    local_deg = jnp.sum(dense.astype(jnp.float32), axis=(2, 3)).reshape(tile_rows_blk * tile)
    grad_own = cotangent[0, 0]
    deg_round = lax.reduce_precision(local_deg, exponent_bits=8, mantissa_bits=7)
    deg_high = deg_round.astype(jnp.bfloat16)
    deg_low = (local_deg - deg_round).astype(jnp.bfloat16)
    extra = jnp.zeros((16, width), jnp.bfloat16)
    extra = extra.at[0:2].set(deg_high.reshape(2, width)).at[2:4].set(deg_low.reshape(2, width))
    payload = jnp.concatenate([grad_own, extra], axis=0)
    spread = jnp.broadcast_to(payload[None], (cols_axis,) + payload.shape)
    got = lax.all_to_all(spread, "col", 0, 0)
    grad_rows = got[:, :sub_rows].reshape(cols_axis * sub_rows, width)
    deg_parts = got[:, sub_rows:sub_rows + 4].astype(jnp.float32)
    deg_all = jnp.sum(deg_parts[:, 0:2] + deg_parts[:, 2:4], axis=0).reshape(-1)
    inv_all = lax.rsqrt(1.0 + deg_all)
    me_col = lax.axis_index("col")
    inv_own = lax.dynamic_slice_in_dim(inv_all, me_col * sub_rows, sub_rows)

    projected = lax.dot_general(
        grad_rows, weight, (((1,), (1,)), ((), ())), preferred_element_type=jnp.float32
    )
    scaled = (inv_all[:, None] * projected).astype(jnp.bfloat16)
    dense_flat = dense.reshape(tile_rows_blk * tile, tile_cols_blk * tile)
    back_t = lax.dot_general(
        scaled, dense_flat, (((0,), (0,)), ((), ())), preferred_element_type=jnp.float32
    )
    half = width // 2
    odd = lax.axis_index("row") % 2 == 1
    low, high = back_t[:half], back_t[half:]
    keep = jnp.where(odd, high, low)
    give = jnp.where(odd, low, high).astype(jnp.bfloat16)
    partner = [(i, i ^ 1) for i in range(rows_axis)]
    chip_sum = keep + lax.ppermute(give, "row", partner).astype(jnp.float32)
    pieces = chip_sum.astype(jnp.bfloat16).T.reshape(rows_axis, sub_rows, half)
    arrived = lax.all_to_all(pieces, "row", 0, 0)
    parity = jnp.arange(rows_axis, dtype=jnp.int32) % 2
    from_even = (parity == 0).astype(jnp.bfloat16)
    from_odd = (parity == 1).astype(jnp.bfloat16)
    grad_low = jnp.einsum("r,rnf->nf", from_even, arrived, preferred_element_type=jnp.float32)
    grad_high = jnp.einsum("r,rnf->nf", from_odd, arrived, preferred_element_type=jnp.float32)
    feature_grad = jnp.concatenate([grad_low, grad_high], axis=1).astype(jnp.bfloat16)

    panel = lax.all_gather(features, "row", axis=1, tiled=True).reshape(tile_cols_blk, tile, width)
    panel, _ = lax.optimization_barrier((panel, pieces))
    total = jnp.einsum("aibj,bjf->aif", dense, panel, preferred_element_type=jnp.float32)
    partial_agg = total.reshape(tile_rows_blk * tile, width)
    scaled_partial = (inv_all[:, None] * partial_agg).astype(jnp.bfloat16)
    weight_term = lax.dot_general(
        scaled_partial, grad_rows, (((0,), (0,)), ((), ())), preferred_element_type=jnp.float32
    )
    weight_term, _ = lax.optimization_barrier((weight_term, arrived))
    summed = lax.psum_scatter(partial_agg, "col", scatter_dimension=0, tiled=True)
    aggregated = (inv_own[:, None] * summed).astype(jnp.bfloat16)
    layer_out = jnp.dot(aggregated, weight, preferred_element_type=jnp.float32).astype(jnp.bfloat16)
    nodes = sub_rows * rows_axis * cols_axis
    weight_pieces = weight_term.astype(jnp.bfloat16).reshape(cols_axis, width // cols_axis, width)
    ones_col = jnp.ones((cols_axis,), jnp.bfloat16)
    weight_part = jnp.einsum(
        "c,cnf->nf", ones_col, lax.all_to_all(weight_pieces, "col", 0, 0),
        preferred_element_type=jnp.float32,
    )
    weight_pieces = weight_part.reshape(rows_axis, width // cols_axis // rows_axis, width)
    weight_part = jnp.sum(lax.all_to_all(weight_pieces, "row", 0, 0), axis=0) * nodes ** (-0.5)
    spread = jnp.broadcast_to(weight_part[None], (rows_axis,) + weight_part.shape)
    weight_part = lax.all_to_all(spread, "row", 0, 0).reshape(width // cols_axis, width)
    spread = jnp.broadcast_to(weight_part[None], (cols_axis,) + weight_part.shape)
    weight_grad = lax.all_to_all(spread, "col", 0, 0).reshape(width, width)
    return (
        layer_out.reshape(1, 1, sub_rows, width),
        weight_grad,
        feature_grad.reshape(1, 1, sub_rows, width),
    )


def solution(mesh):
    return jax.shard_map(
        per_device,
        mesh=mesh,
        in_specs=(
            P("col", "row", None, None),
            P(),
            P("row", "col", None, None),
            P("row", "col", None, None, None),
            P("row", "col", None),
            P("row", "col", None),
            P("row", "col"),
        ),
        out_specs=(P("row", "col", None, None), P(), P("col", "row", None, None)),
        check_vma=False,
    )
```

```python
import jax
import jax.numpy as jnp
from jax import lax
from jax.sharding import PartitionSpec as P


def per_device(features, weight, cotangent, tile_vals, tile_rows, tile_cols, tile_count):
    sub_rows = features.shape[2]
    width = features.shape[3]
    slots = tile_vals.shape[2]
    tile = tile_vals.shape[3]
    rows_axis = lax.axis_size("row")
    cols_axis = lax.axis_size("col")
    tile_rows_blk = sub_rows * cols_axis // tile
    tile_cols_blk = sub_rows * rows_axis // tile
    places = tile_rows_blk * tile_cols_blk

    live = jnp.arange(slots, dtype=jnp.int32) < tile_count[0, 0]
    place = tile_rows[0, 0] * tile_cols_blk + tile_cols[0, 0]
    onehot = (place[:, None] == jnp.arange(places, dtype=jnp.int32)[None, :]) & live[:, None]
    onehot = onehot.astype(jnp.bfloat16).reshape(slots, tile_rows_blk, tile_cols_blk)
    dense = jnp.einsum(
        "kab,kij->aibj", onehot, tile_vals[0, 0], preferred_element_type=jnp.float32
    ).astype(jnp.bfloat16)

    row_sums = jnp.sum(tile_vals[0, 0].astype(jnp.float32), axis=2)
    row_hot = ((tile_rows[0, 0][:, None] == jnp.arange(tile_rows_blk, dtype=jnp.int32)[None, :])
               & live[:, None]).astype(jnp.float32)
    local_deg = jnp.einsum(
        "ka,ki->ai", row_hot, row_sums, precision=lax.Precision.HIGHEST,
        preferred_element_type=jnp.float32,
    ).reshape(tile_rows_blk * tile)
    grad_own = cotangent[0, 0]
    deg_round = lax.reduce_precision(local_deg, exponent_bits=8, mantissa_bits=7)
    deg_high = deg_round.astype(jnp.bfloat16)
    deg_low = (local_deg - deg_round).astype(jnp.bfloat16)
    extra = jnp.zeros((16, width), jnp.bfloat16)
    extra = extra.at[0:2].set(deg_high.reshape(2, width)).at[2:4].set(deg_low.reshape(2, width))
    payload = jnp.concatenate([grad_own, extra], axis=0)
    spread = jnp.broadcast_to(payload[None], (cols_axis,) + payload.shape)
    got = lax.all_to_all(spread, "col", 0, 0)
    grad_rows = got[:, :sub_rows].reshape(cols_axis * sub_rows, width)
    deg_parts = got[:, sub_rows:sub_rows + 4].astype(jnp.float32)
    deg_all = jnp.sum(deg_parts[:, 0:2] + deg_parts[:, 2:4], axis=0).reshape(-1)
    inv_all = lax.rsqrt(1.0 + deg_all)
    me_col = lax.axis_index("col")
    inv_own = lax.dynamic_slice_in_dim(inv_all, me_col * sub_rows, sub_rows)

    projected = lax.dot_general(
        grad_rows, weight, (((1,), (1,)), ((), ())), preferred_element_type=jnp.float32
    )
    scaled = (inv_all[:, None] * projected).astype(jnp.bfloat16)
    dense_flat = dense.reshape(tile_rows_blk * tile, tile_cols_blk * tile)
    back_t = lax.dot_general(
        scaled, dense_flat, (((0,), (0,)), ((), ())), preferred_element_type=jnp.float32
    )
    half = width // 2
    odd = lax.axis_index("row") % 2 == 1
    low, high = back_t[:half], back_t[half:]
    keep = jnp.where(odd, high, low)
    give = jnp.where(odd, low, high)
    partner = [(i, i ^ 1) for i in range(rows_axis)]
    chip_sum = keep + lax.ppermute(give, "row", partner)
    pieces = chip_sum.astype(jnp.bfloat16).T.reshape(rows_axis, sub_rows, half)
    arrived = lax.all_to_all(pieces, "row", 0, 0)
    parity = jnp.arange(rows_axis, dtype=jnp.int32) % 2
    from_even = (parity == 0).astype(jnp.bfloat16)
    from_odd = (parity == 1).astype(jnp.bfloat16)
    grad_low = jnp.einsum("r,rnf->nf", from_even, arrived, preferred_element_type=jnp.float32)
    grad_high = jnp.einsum("r,rnf->nf", from_odd, arrived, preferred_element_type=jnp.float32)
    feature_grad = jnp.concatenate([grad_low, grad_high], axis=1).astype(jnp.bfloat16)

    panel = lax.all_gather(features, "row", axis=1, tiled=True).reshape(tile_cols_blk, tile, width)
    panel, _ = lax.optimization_barrier((panel, pieces))
    total = jnp.einsum("aibj,bjf->aif", dense, panel, preferred_element_type=jnp.float32)
    partial_agg = total.reshape(tile_rows_blk * tile, width)
    scaled_partial = (inv_all[:, None] * partial_agg).astype(jnp.bfloat16)
    weight_term = lax.dot_general(
        scaled_partial, grad_rows, (((0,), (0,)), ((), ())), preferred_element_type=jnp.float32
    )
    weight_term, _ = lax.optimization_barrier((weight_term, arrived))
    summed = lax.psum_scatter(partial_agg, "col", scatter_dimension=0, tiled=True)
    aggregated = (inv_own[:, None] * summed).astype(jnp.bfloat16)
    layer_out = jnp.dot(aggregated, weight, preferred_element_type=jnp.float32).astype(jnp.bfloat16)
    nodes = sub_rows * rows_axis * cols_axis
    weight_pieces = weight_term.astype(jnp.bfloat16).reshape(cols_axis, width // cols_axis, width)
    ones_col = jnp.ones((cols_axis,), jnp.bfloat16)
    weight_part = jnp.einsum(
        "c,cnf->nf", ones_col, lax.all_to_all(weight_pieces, "col", 0, 0),
        preferred_element_type=jnp.float32,
    )
    weight_pieces = weight_part.reshape(rows_axis, width // cols_axis // rows_axis, width)
    weight_part = jnp.sum(lax.all_to_all(weight_pieces, "row", 0, 0), axis=0) * nodes ** (-0.5)
    spread = jnp.broadcast_to(weight_part[None], (rows_axis,) + weight_part.shape)
    weight_part = lax.all_to_all(spread, "row", 0, 0).reshape(width // cols_axis, width)
    spread = jnp.broadcast_to(weight_part[None], (cols_axis,) + weight_part.shape)
    weight_grad = lax.all_to_all(spread, "col", 0, 0).reshape(width, width)
    return (
        layer_out.reshape(1, 1, sub_rows, width),
        weight_grad,
        feature_grad.reshape(1, 1, sub_rows, width),
    )


def solution(mesh):
    return jax.shard_map(
        per_device,
        mesh=mesh,
        in_specs=(
            P("col", "row", None, None),
            P(),
            P("row", "col", None, None),
            P("row", "col", None, None, None),
            P("row", "col", None),
            P("row", "col", None),
            P("row", "col"),
        ),
        out_specs=(P("row", "col", None, None), P(), P("col", "row", None, None)),
        check_vma=False,
    )
```
